256 devices in a mesh: rep: 2 (over core), ep: 128 (over z, y, x).
Axes of the slice: x: 4, y: 4, z: 8, core: 2. Of those that a mesh axis runs over, the one named last changes fastest.
Arguments:
- resid_in: bfloat16 [16384, 2048], P(('rep', 'ep')), may hold values from -6 to 6
- context: bfloat16 [16384, 2048], P('rep', 'ep'), may hold values from -24 to 24
- out_proj: bfloat16 [2048, 2048], P('ep'), may hold values from -0.125 to 0.125
- norm_gain: float32 [2048], replicated, may hold values from 0.5 to 1.5
- router: bfloat16 [2048, 64], replicated, may hold values from -0.03125 to 0.03125
- routes: int32 [16384, 8], P(('rep', 'ep')), may hold values from 0 to 63, all different within a row; in each aligned block of 64 rows (0 to 63, 64 to 127, ...) at most 10 rows name the same one
- w_gate: bfloat16 [2048, 65536], P(None, ('rep', 'ep')), may hold values from -0.125 to 0.125
- w_up: bfloat16 [2048, 65536], P(None, ('rep', 'ep')), may hold values from -0.125 to 0.125
- w_down: bfloat16 [65536, 2048], P(('rep', 'ep')), may hold values from -0.5 to 0.5
- next_gain: float32 [2048], replicated, may hold values from 0.5 to 1.5
Outputs:
- resid_out: bfloat16 [16384, 2048], P(('rep', 'ep'))
- next_normed: bfloat16 [16384, 2048], P(('rep', 'ep'))
The draws below stay inside these ranges and needn't reach their ends.
Inputs may be any that keep to these rules, and one draw needn't show every extreme that they name: `routes`: each row names 8 different experts. Among the 64 rows of one device no expert is named by more than 10 rows, a bound that some block reaches.
All inputs are finite; a program needn't handle non-finite values.
Results may differ from the reference program's by a relative error of at most 0.014.
Values may be sent and summed in bfloat16 or wider, within the bound.
No kernel may reach another device: no remote copies, remote signals or barrier semaphores. Data moves between devices by JAX's collectives and lax.ppermute only.
A program may use at most 192 MiB of HBM per device.

```python
import math
import jax
import jax.numpy as jnp
import numpy as np
from jax import lax

D = 2048
ATT = 2048
EXPERTS = 64
FF_E = 1024
TOP = 8
TOK_DEV = 64
MOST = 10
TOKENS = 16384
UNITS = 256


def spiked(array, rng, source, target, blocks, factor):
    owner, partner = [(jnp.arange(array.shape[axis_at]) // (array.shape[axis_at] // blocks)).reshape([-1 if axis == axis_at else 1 for axis in range(array.ndim)]) for axis_at in (source, target)]
    chosen = jax.random.permutation(rng, blocks)[partner]
    strong = (owner == chosen) | (owner == (partner + blocks // 2) % blocks)
    return jnp.where(strong, factor * array, array)


def shard_levels(own_key, shape, split, low, high):
    level = 1.0
    for position, shards_of in split:
        heights = jax.random.uniform(jax.random.fold_in(jax.random.fold_in(own_key, 6), position), (shards_of,), jnp.float32, low / len(split), high / len(split))
        level = level * jnp.repeat(jnp.exp(heights), shape[position] // shards_of).reshape((-1,) + (1,) * (len(shape) - 1 - position))
    return level


def routed_block(stream_key, own, number, rows, amount, top, reach, lean):
    order = jax.random.permutation(stream_key, amount)
    heavy_load, common = shares(amount, rows * top, reach, lean, True), shares(amount, rows * top, reach, lean, False)
    places = jnp.arange(amount)

    def named(sizes, turn):
        used = int((sizes > 0).sum())
        fixed = max(1, used // 4)
        passed = fixed + (places - fixed + turn * (used - fixed)) % max(1, amount - fixed)
        return jnp.zeros((amount,), jnp.int32).at[order[jnp.where(places < fixed, places, passed)]].set(jnp.asarray(sizes, jnp.int32))

    sizes = jnp.where(number % 4 == 0, named(heavy_load, number // 4), named(common, number - number // 4 - 1))
    mixed = jax.random.permutation(jax.random.fold_in(own, 3), amount)
    giver, sink = mixed[0:amount // 2 * 2:2], mixed[1:amount // 2 * 2:2]
    room = jnp.minimum(sizes[giver] - 1, reach - sizes[sink]) // 2
    room = jnp.where((giver == order[0]) | (sink == order[0]) | (sizes[sink] == 0), 0, jnp.maximum(room, 0))
    passed = jax.random.randint(jax.random.fold_in(own, 4), (amount // 2,), 0, 1 << 20) % (room + 1)
    sizes = sizes.at[giver].add(-passed).at[sink].add(passed)
    members = jnp.searchsorted(jnp.cumsum(sizes), jnp.arange(rows * top), side="right").astype(jnp.int32)
    table = members.reshape(top, rows).T
    table = table[jax.random.permutation(jax.random.fold_in(own, 1), rows)]
    turn = jax.random.randint(jax.random.fold_in(own, 2), (rows, 1), 0, top)
    return jnp.take_along_axis(table, (jnp.arange(top)[None, :] + turn) % top, axis=1)


def shares(number_of, total, most, skew, full):
    loads = [(1 << 20) // math.isqrt(standing ** skew) + 1 for standing in range(1, number_of + 1)]
    largest = most if full else min(most, max(-(-total // number_of), total * loads[0] // sum(loads)))
    least = 1 if total - largest >= number_of - 1 else 0
    given, spare = [largest] + [least] * (number_of - 1), total - largest - least * (number_of - 1)
    while spare > 0:
        movable = [i for i in range(1, number_of) if given[i] < largest] or [i for i in range(1, number_of) if given[i] < most]
        pool, left = sum([loads[i] for i in movable]), spare
        for i in movable:
            more = min(most - given[i], max(1, left * loads[i] // pool), spare)
            given[i] = given[i] + more
            spare = spare - more
    return np.array(given)


def scatter_about(key, dims, width, limit, split=(), held_as=jnp.bfloat16):
    values = width * jax.random.normal(key, dims, jnp.float32)
    if split:
        values = values * shard_levels(key, dims, split, -0.22, 0.18)
    return jnp.clip(values, -limit, limit).astype(held_as)


def gaussian_with(key, shape, deviation, limit, shards, heavy, kind=jnp.bfloat16):
    result = deviation * jax.random.normal(key, shape, jnp.float32)
    if shards:
        result = result * shard_levels(key, shape, shards, -0.22, 0.18)
    return jnp.clip(spiked(result, jax.random.fold_in(key, 3), *heavy), -limit, limit).astype(kind)


def setup_inputs(seed: int = 0) -> dict:
    arg_keys = jax.random.split(jax.random.key(seed), 11)
    resid_in = scatter_about(arg_keys[0], (TOKENS, D), 1.0, 6.0, ((0, 256),))
    context = gaussian_with(arg_keys[1], (TOKENS, ATT), 1.0, 24.0, ((0, 2), (1, 128)), (1, 0, 128, 5.5))
    out_proj = scatter_about(arg_keys[2], (ATT, D), ATT ** -0.5, 0.125, ((0, 128),))
    norm_gain = jnp.clip(1.0 + 0.1 * jax.random.normal(arg_keys[3], (D,), jnp.float32), 0.5, 1.5)
    router = scatter_about(arg_keys[4], (D, EXPERTS), (16 * D) ** -0.5, 0.03125)
    routes_keys = jax.random.split(jax.random.fold_in(arg_keys[5], 1), TOKENS // TOK_DEV)
    routes_turns = jax.random.permutation(jax.random.fold_in(arg_keys[5], 3), TOKENS // TOK_DEV)
    routes = jax.vmap(lambda own, number: routed_block(jax.random.fold_in(arg_keys[5], 2), own, number, TOK_DEV, EXPERTS, TOP, MOST, 2))(routes_keys, routes_turns).reshape((TOKENS, TOP))
    w_gate = scatter_about(arg_keys[6], (D, EXPERTS * FF_E), D ** -0.5, 0.125, ((1, 256),))
    w_up = scatter_about(arg_keys[7], (D, EXPERTS * FF_E), D ** -0.5, 0.125, ((1, 256),))
    w_down = scatter_about(arg_keys[8], (EXPERTS * FF_E, D), (FF_E // 9) ** -0.5, 0.5, ((0, 256),))
    next_gain = jnp.clip(1.0 + 0.1 * jax.random.normal(arg_keys[9], (D,), jnp.float32), 0.5, 1.5)
    return {"resid_in": resid_in, "context": context, "out_proj": out_proj, "norm_gain": norm_gain, "router": router, "routes": routes, "w_gate": w_gate, "w_up": w_up, "w_down": w_down, "next_gain": next_gain}


def rms_norm(values, gain_row):
    widened = values.astype(jnp.float32)
    factor = lax.rsqrt(lax.optimization_barrier(jnp.mean(widened * widened, axis=-1, keepdims=True)) + 1e-06)
    return (widened * factor * gain_row).astype(jnp.bfloat16)

def reference(resid_in, context, out_proj, norm_gain, router, routes, w_gate, w_up, w_down, next_gain):
    attention = jnp.dot(context, out_proj, preferred_element_type=jnp.float32)
    hidden = (resid_in.astype(jnp.float32) + attention).astype(jnp.bfloat16)
    normed = rms_norm(hidden, norm_gain)
    logits = jnp.dot(normed, router, preferred_element_type=jnp.float32)
    picked = jnp.take_along_axis(logits, routes, axis=1)
    raised = jnp.exp(picked)
    route_weight = (raised / lax.optimization_barrier(jnp.sum(raised, axis=1, keepdims=True))).astype(jnp.bfloat16)
    flat_weight = route_weight.reshape(-1)
    flat_routes = routes.reshape(-1).astype(jnp.int32)
    sorted_order = jnp.argsort(flat_routes, stable=True).astype(jnp.int32)
    counts = lax.optimization_barrier(jnp.sum((flat_routes[:, None] == jnp.arange(EXPERTS, dtype=jnp.int32)[None, :]).astype(jnp.int32), axis=0)).astype(jnp.int32)
    starts = (jnp.cumsum(counts) - counts).astype(jnp.int32)
    window = MOST * (TOKENS // TOK_DEV)
    padded = jnp.concatenate([sorted_order, jnp.zeros((window,), jnp.int32)])
    block_size = min(UNITS, FF_E)
    block_count = FF_E // block_size

    def one_expert(expert_id, running):
        expert_id = jnp.asarray(expert_id).astype(jnp.int32)
        picked_index = lax.dynamic_slice_in_dim(padded, starts[expert_id].astype(jnp.int32), window)
        live_rows = jnp.arange(window, dtype=jnp.int32) < counts[expert_id]
        token_index = (picked_index // TOP).astype(jnp.int32)
        token_rows = normed[token_index]
        first = (expert_id * FF_E).astype(jnp.int32)
        gate_cols = lax.dynamic_slice_in_dim(w_gate, first, FF_E, 1)
        up_cols = lax.dynamic_slice_in_dim(w_up, first, FF_E, 1)
        down_rows = lax.dynamic_slice_in_dim(w_down, first, FF_E, 0)
        gate_h = jnp.dot(token_rows, gate_cols, preferred_element_type=jnp.float32)
        up_h = jnp.dot(token_rows, up_cols, preferred_element_type=jnp.float32)
        activated = (jax.nn.silu(gate_h) * up_h).astype(jnp.bfloat16)
        partials = jnp.einsum('rbf,bfd->rbd', activated.reshape(window, block_count, block_size).astype(jnp.float32), down_rows.reshape(block_count, block_size, D).astype(jnp.float32)).astype(jnp.bfloat16)
        weighted = jnp.where(live_rows, flat_weight[picked_index].astype(jnp.float32), jnp.float32(0.0))
        addition = lax.optimization_barrier(jnp.sum(partials.astype(jnp.float32), axis=1)) * weighted[:, None]
        return running.at[token_index].add(addition)
    expert_sum = lax.fori_loop(0, EXPERTS, one_expert, jnp.zeros((TOKENS, D), jnp.float32))
    resid_out = (hidden.astype(jnp.float32) + expert_sum).astype(jnp.bfloat16)
    next_normed = rms_norm(resid_out, next_gain)
    return (resid_out, next_normed)
```

```python
import jax
import jax.numpy as jnp
from jax import lax
from jax.sharding import Mesh
from jax.sharding import PartitionSpec as P

FF_E = 1024
MOST = 10


def rms_norm(values, gain_row):
    widened = values.astype(jnp.float32)
    factor = lax.rsqrt(jnp.mean(widened * widened, axis=-1, keepdims=True) + 1e-06)
    return (widened * factor * gain_row).astype(jnp.bfloat16)


def body(resid_in, context, out_proj, norm_gain, router, routes, w_gate, w_up, w_down, next_gain):
    model_width = resid_in.shape[1]
    tokens = resid_in.shape[0]
    rep_count = lax.axis_size("rep")
    rep_id = lax.axis_index("rep")

    token_ctx = lax.all_to_all(context, ("grp", "q"), split_axis=0, concat_axis=1, tiled=True)
    half = model_width // rep_count
    proj_half = lax.dynamic_slice_in_dim(out_proj, rep_id * half, half, axis=1)
    proj_cols = lax.all_gather(proj_half, ("grp", "q"), axis=0, tiled=True)
    chip_ctx = lax.all_gather(token_ctx, "rep", axis=0, tiled=True)
    att_cols = jnp.dot(chip_ctx, proj_cols, preferred_element_type=jnp.float32)
    att_cols = att_cols.reshape(rep_count, tokens, half)
    attention = lax.all_to_all(att_cols, "rep", split_axis=0, concat_axis=2, tiled=True)
    attention = attention.reshape(tokens, model_width)

    hidden = (resid_in.astype(jnp.float32) + attention).astype(jnp.bfloat16)
    normed = rms_norm(hidden, norm_gain)
    logits = jnp.dot(normed, router, preferred_element_type=jnp.float32)
    experts = router.shape[1]
    picked_mask = (
        routes[:, :, None] == jnp.arange(experts, dtype=jnp.int32)[None, None, :]
    ).astype(jnp.int32)
    picked = jnp.sum(picked_mask.astype(jnp.float32) * logits[:, None, :], axis=2)
    raised = jnp.exp(picked)
    route_weight = (raised / jnp.sum(raised, axis=1, keepdims=True)).astype(jnp.bfloat16)

    named_count = jnp.sum(picked_mask, axis=1)
    before = jnp.cumsum(named_count, axis=0) - named_count
    order_rank = jnp.sum(picked_mask * before[:, None, :], axis=2)
    slot_index = routes * MOST + order_rank
    slot_total = experts * MOST
    slot_hits = slot_index[None] == jnp.arange(slot_total, dtype=jnp.int32)[:, None, None]
    placing = jnp.any(slot_hits, axis=2).astype(jnp.bfloat16)
    outgoing = jnp.dot(placing, normed, preferred_element_type=jnp.bfloat16)
    outgoing = outgoing.reshape(experts, MOST, model_width)
    arrived = lax.all_to_all(outgoing, ("rep", "grp"), split_axis=0, concat_axis=0, tiled=True)
    rows = arrived.reshape(-1, model_width)

    gate_full = lax.all_gather(w_gate, "q", axis=1, tiled=True)
    up_full = lax.all_gather(w_up, "q", axis=1, tiled=True)
    down_full = lax.all_gather(w_down, "q", axis=0, tiled=True)
    block_size = w_gate.shape[1]
    block_count = FF_E // block_size
    gate_h = jnp.dot(rows, gate_full, preferred_element_type=jnp.float32)
    up_h = jnp.dot(rows, up_full, preferred_element_type=jnp.float32)
    activated = (jax.nn.silu(gate_h) * up_h).astype(jnp.bfloat16)
    produced = jnp.einsum(
        "sbf,bfd->sbd",
        activated.reshape(-1, block_count, block_size),
        down_full.reshape(block_count, block_size, model_width),
        preferred_element_type=jnp.float32,
    ).astype(jnp.bfloat16)
    summed = jnp.sum(produced.astype(jnp.float32), axis=1).astype(jnp.bfloat16)
    summed = summed.reshape(experts, MOST, model_width)
    returned = lax.all_to_all(summed, ("rep", "grp"), split_axis=0, concat_axis=0, tiled=True)
    returned = returned.reshape(slot_total, model_width)

    weighing = jnp.sum(
        slot_hits.astype(jnp.float32) * route_weight.astype(jnp.float32)[None], axis=2
    ).T.astype(jnp.bfloat16)
    expert_sum = jnp.dot(weighing, returned, preferred_element_type=jnp.float32)
    resid_out = (hidden.astype(jnp.float32) + expert_sum).astype(jnp.bfloat16)
    next_normed = rms_norm(resid_out, next_gain)
    return (resid_out, next_normed)


def solution(mesh):
    rep_count = mesh.shape["rep"]
    ep_count = mesh.shape["ep"]
    units = 65536 // (rep_count * ep_count)
    owners = max(FF_E // units, 1)
    devices = mesh.devices.reshape(rep_count, ep_count // owners, owners)
    grid = Mesh(devices, ("rep", "grp", "q"))
    tok = ("rep", "grp", "q")
    feat = ("grp", "q")
    in_specs = (
        P(tok, None),
        P("rep", feat),
        P(feat, None),
        P(),
        P(),
        P(tok, None),
        P(None, tok),
        P(None, tok),
        P(tok, None),
        P(),
    )
    out_specs = (P(tok, None), P(tok, None))
    return jax.shard_map(body, mesh=grid, in_specs=in_specs, out_specs=out_specs, check_vma=False)
```

```python
import jax
import jax.numpy as jnp
from jax import lax
from jax.sharding import Mesh
from jax.sharding import PartitionSpec as P

FF_E = 1024
MOST = 10


def rms_norm(values, gain_row):
    widened = values.astype(jnp.float32)
    factor = lax.rsqrt(jnp.mean(widened * widened, axis=-1, keepdims=True) + 1e-06)
    return (widened * factor * gain_row).astype(jnp.bfloat16)


def shift_pairs(size, offset):
    return [(i, (i + offset) % size) for i in range(size)]


def gather_proj(block, sizes):
    x_n, z_n, y_n = sizes["x"], sizes["z"], sizes["y"]
    parts = [block] + [lax.ppermute(block, "x", shift_pairs(x_n, d)) for d in range(1, x_n)]
    block = jnp.stack(parts)
    parts = [block] + [lax.ppermute(block, "z", shift_pairs(z_n, d)) for d in range(1, z_n)]
    block = jnp.stack(parts)
    if y_n == 4:
        ahead = lax.ppermute(block, "y", shift_pairs(4, 1))
        behind = lax.ppermute(block, "y", shift_pairs(4, 3))
        cut = block.shape[0] // 2
        far_a = lax.ppermute(ahead[:cut], "y", shift_pairs(4, 1))
        far_b = lax.ppermute(behind[cut:], "y", shift_pairs(4, 3))
        parts = [block, ahead, jnp.concatenate([far_a, far_b]), behind]
    else:
        parts = [block] + [lax.ppermute(block, "y", shift_pairs(y_n, d)) for d in range(1, y_n)]
    return jnp.stack(parts)


def body(resid_in, context, out_proj, norm_gain, router, routes, w_gate, w_up, w_down, next_gain):
    model_width = resid_in.shape[1]
    tokens = resid_in.shape[0]
    sizes = {a: lax.axis_size(a) for a in ("rep", "z", "y", "x")}
    rep_count = sizes["rep"]
    rep_id = lax.axis_index("rep")
    chip = ("z", "y", "x")

    combo = jnp.concatenate([w_gate, w_up, w_down.T], axis=1)
    combo_all = lax.all_gather(combo, "x", axis=0, tiled=False)

    token_ctx = lax.all_to_all(context, chip, split_axis=0, concat_axis=1, tiled=True)
    half = model_width // rep_count
    proj_half = lax.dynamic_slice_in_dim(out_proj, rep_id * half, half, axis=1)
    proj_rows = gather_proj(proj_half, sizes)
    feat_block = proj_half.shape[0]
    proj_rows = proj_rows.reshape(-1, half)
    dy = jnp.arange(sizes["y"])[:, None, None]
    dz = jnp.arange(sizes["z"])[None, :, None]
    dx = jnp.arange(sizes["x"])[None, None, :]
    src = (
        ((lax.axis_index("z") - dz) % sizes["z"]) * (sizes["y"] * sizes["x"])
        + ((lax.axis_index("y") - dy) % sizes["y"]) * sizes["x"]
        + (lax.axis_index("x") - dx) % sizes["x"]
    ).reshape(-1)
    chip_ctx = lax.all_gather(token_ctx, "rep", axis=0, tiled=True)
    chip_ctx = chip_ctx.reshape(chip_ctx.shape[0], -1, feat_block)
    chip_ctx = jnp.take(chip_ctx, src, axis=1).reshape(chip_ctx.shape[0], -1)
    att_cols = jnp.dot(chip_ctx, proj_rows, preferred_element_type=jnp.float32)
    att_cols = att_cols.reshape(rep_count, tokens, half)
    attention = lax.all_to_all(att_cols, "rep", split_axis=0, concat_axis=2, tiled=True)
    attention = attention.reshape(tokens, model_width)

    hidden = (resid_in.astype(jnp.float32) + attention).astype(jnp.bfloat16)
    normed = rms_norm(hidden, norm_gain)
    logits = jnp.dot(normed, router, preferred_element_type=jnp.float32)
    experts = router.shape[1]
    picked_mask = (
        routes[:, :, None] == jnp.arange(experts, dtype=jnp.int32)[None, None, :]
    ).astype(jnp.int32)
    picked = jnp.sum(picked_mask.astype(jnp.float32) * logits[:, None, :], axis=2)
    raised = jnp.exp(picked)
    route_weight = (raised / jnp.sum(raised, axis=1, keepdims=True)).astype(jnp.bfloat16)

    named_count = jnp.sum(picked_mask, axis=1)
    before = jnp.cumsum(named_count, axis=0) - named_count
    order_rank = jnp.sum(picked_mask * before[:, None, :], axis=2)
    slot_index = routes * MOST + order_rank
    slot_total = experts * MOST
    slot_hits = slot_index[None] == jnp.arange(slot_total, dtype=jnp.int32)[:, None, None]
    placing = jnp.any(slot_hits, axis=2).astype(jnp.bfloat16)
    outgoing = jnp.dot(placing, normed, preferred_element_type=jnp.bfloat16)
    outgoing = outgoing.reshape(experts, MOST, model_width)
    arrived = lax.all_to_all(outgoing, ("rep", "z", "y"), split_axis=0, concat_axis=0, tiled=True)
    rows = arrived.reshape(-1, model_width)

    block_size = w_gate.shape[1]
    gate_all = combo_all[:, :, :block_size]
    up_all = combo_all[:, :, block_size:2 * block_size]
    down_all = combo_all[:, :, 2 * block_size:]
    gate_h = jnp.einsum("sd,qdj->sqj", rows, gate_all, preferred_element_type=jnp.float32)
    up_h = jnp.einsum("sd,qdj->sqj", rows, up_all, preferred_element_type=jnp.float32)
    activated = (jax.nn.silu(gate_h) * up_h).astype(jnp.bfloat16)
    produced = jnp.einsum(
        "sqj,qdj->sqd", activated, down_all, preferred_element_type=jnp.float32
    ).astype(jnp.bfloat16)
    summed = jnp.sum(produced.astype(jnp.float32), axis=1).astype(jnp.bfloat16)
    summed = summed.reshape(experts, MOST, model_width)
    returned = lax.all_to_all(summed, ("rep", "z", "y"), split_axis=0, concat_axis=0, tiled=True)
    returned = returned.reshape(slot_total, model_width)

    weighing = jnp.sum(
        slot_hits.astype(jnp.float32) * route_weight.astype(jnp.float32)[None], axis=2
    ).T.astype(jnp.bfloat16)
    expert_sum = jnp.dot(weighing, returned, preferred_element_type=jnp.float32)
    resid_out = (hidden.astype(jnp.float32) + expert_sum).astype(jnp.bfloat16)
    next_normed = rms_norm(resid_out, next_gain)
    return (resid_out, next_normed)


def solution(mesh):
    rep_count = mesh.shape["rep"]
    ep_count = mesh.shape["ep"]
    units = 65536 // (rep_count * ep_count)
    owners = max(FF_E // units, 1)
    rows_of = 4 if (ep_count // owners) % 4 == 0 else 1
    devices = mesh.devices.reshape(rep_count, ep_count // owners // rows_of, rows_of, owners)
    grid = Mesh(devices, ("rep", "z", "y", "x"))
    tok = ("rep", "z", "y", "x")
    feat = ("z", "y", "x")
    in_specs = (
        P(tok, None),
        P("rep", feat),
        P(feat, None),
        P(),
        P(),
        P(tok, None),
        P(None, tok),
        P(None, tok),
        P(tok, None),
        P(),
    )
    out_specs = (P(tok, None), P(tok, None))
    return jax.shard_map(body, mesh=grid, in_specs=in_specs, out_specs=out_specs, check_vma=False)
```

```python
import jax
import jax.numpy as jnp
from jax import lax
from jax.sharding import Mesh
from jax.sharding import PartitionSpec as P

FF_E = 1024
MOST = 10


def rms_norm(values, gain_row):
    widened = values.astype(jnp.float32)
    factor = lax.rsqrt(jnp.mean(widened * widened, axis=-1, keepdims=True) + 1e-06)
    return (widened * factor * gain_row).astype(jnp.bfloat16)


def shift_pairs(size, offset):
    return [(i, (i + offset) % size) for i in range(size)]


def gather_proj(block, sizes):
    x_n, z_n, y_n = sizes["x"], sizes["z"], sizes["y"]
    parts = [block] + [lax.ppermute(block, "x", shift_pairs(x_n, d)) for d in range(1, x_n)]
    block = jnp.stack(parts)
    parts = [block] + [lax.ppermute(block, "z", shift_pairs(z_n, d)) for d in range(1, z_n)]
    block = jnp.stack(parts)
    if y_n == 4:
        ahead = lax.ppermute(block, "y", shift_pairs(4, 1))
        behind = lax.ppermute(block, "y", shift_pairs(4, 3))
        cut = block.shape[0] // 2
        far_a = lax.ppermute(ahead[:cut], "y", shift_pairs(4, 1))
        far_b = lax.ppermute(behind[cut:], "y", shift_pairs(4, 3))
        parts = [block, ahead, jnp.concatenate([far_a, far_b]), behind]
    else:
        parts = [block] + [lax.ppermute(block, "y", shift_pairs(y_n, d)) for d in range(1, y_n)]
    return jnp.stack(parts)


def body(resid_in, context, out_proj, norm_gain, router, routes, w_gate, w_up, w_down, next_gain):
    model_width = resid_in.shape[1]
    tokens = resid_in.shape[0]
    sizes = {a: lax.axis_size(a) for a in ("rep", "z", "y", "x")}
    rep_count = sizes["rep"]
    rep_id = lax.axis_index("rep")
    chip = ("z", "y", "x")

    gate_up = jnp.concatenate([w_gate, w_up], axis=1)
    gate_up_all = lax.all_gather(gate_up, "x", axis=1, tiled=True)
    down_all = lax.all_gather(w_down, "x", axis=0, tiled=True)

    token_ctx = lax.all_to_all(context, chip, split_axis=0, concat_axis=1, tiled=True)
    half = model_width // rep_count
    proj_half = lax.dynamic_slice_in_dim(out_proj, rep_id * half, half, axis=1)
    proj_rows = gather_proj(proj_half, sizes)
    feat_block = proj_half.shape[0]
    proj_rows = proj_rows.reshape(-1, half)
    dy = jnp.arange(sizes["y"])[:, None, None]
    dz = jnp.arange(sizes["z"])[None, :, None]
    dx = jnp.arange(sizes["x"])[None, None, :]
    src = (
        ((lax.axis_index("z") - dz) % sizes["z"]) * (sizes["y"] * sizes["x"])
        + ((lax.axis_index("y") - dy) % sizes["y"]) * sizes["x"]
        + (lax.axis_index("x") - dx) % sizes["x"]
    ).reshape(-1)
    chip_ctx = lax.all_gather(token_ctx, "rep", axis=0, tiled=True)
    chip_ctx = chip_ctx.reshape(chip_ctx.shape[0], -1, feat_block)
    chip_ctx = jnp.take(chip_ctx, src, axis=1).reshape(chip_ctx.shape[0], -1)
    att_cols = jnp.dot(chip_ctx, proj_rows, preferred_element_type=jnp.float32)
    att_cols = att_cols.reshape(rep_count, tokens, half)
    attention = lax.all_to_all(att_cols, "rep", split_axis=0, concat_axis=2, tiled=True)
    attention = attention.reshape(tokens, model_width)

    hidden = (resid_in.astype(jnp.float32) + attention).astype(jnp.bfloat16)
    normed = rms_norm(hidden, norm_gain)
    logits = jnp.dot(normed, router, preferred_element_type=jnp.float32)
    experts = router.shape[1]
    picked_mask = (
        routes[:, :, None] == jnp.arange(experts, dtype=jnp.int32)[None, None, :]
    ).astype(jnp.int32)
    picked = jnp.sum(picked_mask.astype(jnp.float32) * logits[:, None, :], axis=2)
    raised = jnp.exp(picked)
    route_weight = (raised / jnp.sum(raised, axis=1, keepdims=True)).astype(jnp.bfloat16)

    named_count = jnp.sum(picked_mask, axis=1)
    before = jnp.cumsum(named_count, axis=0) - named_count
    order_rank = jnp.sum(picked_mask * before[:, None, :], axis=2)
    slot_index = routes * MOST + order_rank
    slot_total = experts * MOST
    slot_hits = slot_index[None] == jnp.arange(slot_total, dtype=jnp.int32)[:, None, None]
    placing = jnp.any(slot_hits, axis=2).astype(jnp.bfloat16)
    outgoing = jnp.dot(placing, normed, preferred_element_type=jnp.bfloat16)
    outgoing = outgoing.reshape(experts, MOST, model_width)
    outgoing = outgoing.reshape(rep_count, -1, MOST, model_width)
    arrived = lax.all_to_all(outgoing, "rep", split_axis=0, concat_axis=0, tiled=True)
    arrived = jnp.swapaxes(arrived, 0, 1)
    arrived = lax.all_to_all(arrived, ("z", "y"), split_axis=0, concat_axis=0, tiled=True)
    rows = arrived.reshape(-1, model_width)

    block_size = w_gate.shape[1]
    quarters = sizes["x"]
    both = jnp.dot(rows, gate_up_all, preferred_element_type=jnp.float32)
    both = both.reshape(-1, quarters, 2, block_size)
    activated = (jax.nn.silu(both[:, :, 0]) * both[:, :, 1]).astype(jnp.bfloat16)
    produced = jnp.einsum(
        "sqj,qjd->sqd",
        activated,
        down_all.reshape(quarters, block_size, model_width),
        preferred_element_type=jnp.float32,
    ).astype(jnp.bfloat16)
    summed = jnp.sum(produced.astype(jnp.float32), axis=1).astype(jnp.bfloat16)
    summed = summed.reshape(arrived.shape)
    back = lax.all_to_all(summed, ("z", "y"), split_axis=0, concat_axis=0, tiled=True)
    back = jnp.swapaxes(back, 0, 1)
    returned = lax.all_to_all(back, "rep", split_axis=0, concat_axis=0, tiled=True)
    returned = returned.reshape(slot_total, model_width)

    weighing = jnp.sum(
        slot_hits.astype(jnp.float32) * route_weight.astype(jnp.float32)[None], axis=2
    ).T.astype(jnp.bfloat16)
    expert_sum = jnp.dot(weighing, returned, preferred_element_type=jnp.float32)
    resid_out = (hidden.astype(jnp.float32) + expert_sum).astype(jnp.bfloat16)
    next_normed = rms_norm(resid_out, next_gain)
    return (resid_out, next_normed)


def solution(mesh):
    rep_count = mesh.shape["rep"]
    ep_count = mesh.shape["ep"]
    units = 65536 // (rep_count * ep_count)
    owners = max(FF_E // units, 1)
    rows_of = 4 if (ep_count // owners) % 4 == 0 else 1
    devices = mesh.devices.reshape(rep_count, ep_count // owners // rows_of, rows_of, owners)
    grid = Mesh(devices, ("rep", "z", "y", "x"))
    tok = ("rep", "z", "y", "x")
    feat = ("z", "y", "x")
    in_specs = (
        P(tok, None),
        P("rep", feat),
        P(feat, None),
        P(),
        P(),
        P(tok, None),
        P(None, tok),
        P(None, tok),
        P(tok, None),
        P(),
    )
    out_specs = (P(tok, None), P(tok, None))
    return jax.shard_map(body, mesh=grid, in_specs=in_specs, out_specs=out_specs, check_vma=False)
```

```python
import jax
import jax.numpy as jnp
from jax import lax
from jax.sharding import Mesh
from jax.sharding import PartitionSpec as P

FF_E = 1024
MOST = 10


def rms_norm(values, gain_row):
    widened = values.astype(jnp.float32)
    factor = lax.rsqrt(jnp.mean(widened * widened, axis=-1, keepdims=True) + 1e-06)
    return (widened * factor * gain_row).astype(jnp.bfloat16)


def shift_pairs(size, offset):
    return [(i, (i + offset) % size) for i in range(size)]


def gather_proj(block, sizes):
    x_n, z_n, y_n = sizes["x"], sizes["z"], sizes["y"]
    parts = [block] + [lax.ppermute(block, "x", shift_pairs(x_n, d)) for d in range(1, x_n)]
    block = jnp.stack(parts)
    parts = [block] + [lax.ppermute(block, "z", shift_pairs(z_n, d)) for d in range(1, z_n)]
    block = jnp.stack(parts)
    if y_n == 4:
        ahead = lax.ppermute(block, "y", shift_pairs(4, 1))
        behind = lax.ppermute(block, "y", shift_pairs(4, 3))
        cut = block.shape[0] // 2
        far_a = lax.ppermute(ahead[:cut], "y", shift_pairs(4, 1))
        far_b = lax.ppermute(behind[cut:], "y", shift_pairs(4, 3))
        parts = [block, ahead, jnp.concatenate([far_a, far_b]), behind]
    else:
        parts = [block] + [lax.ppermute(block, "y", shift_pairs(y_n, d)) for d in range(1, y_n)]
    return jnp.stack(parts)


def body(resid_in, context, out_proj, norm_gain, router, routes, w_gate, w_up, w_down, next_gain):
    model_width = resid_in.shape[1]
    tokens = resid_in.shape[0]
    sizes = {a: lax.axis_size(a) for a in ("rep", "z", "y", "x")}
    rep_count = sizes["rep"]
    rep_id = lax.axis_index("rep")
    chip = ("z", "y", "x")

    gate_all = lax.all_gather(w_gate, "x", axis=1, tiled=True)
    up_all = lax.all_gather(w_up, "x", axis=1, tiled=True)
    down_all = lax.all_gather(w_down, "x", axis=0, tiled=True)

    token_ctx = lax.all_to_all(context, chip, split_axis=0, concat_axis=1, tiled=True)
    half = model_width // rep_count
    proj_half = lax.dynamic_slice_in_dim(out_proj, rep_id * half, half, axis=1)
    proj_rows = gather_proj(proj_half, sizes)
    feat_block = proj_half.shape[0]
    proj_rows = proj_rows.reshape(-1, half)
    dy = jnp.arange(sizes["y"])[:, None, None]
    dz = jnp.arange(sizes["z"])[None, :, None]
    dx = jnp.arange(sizes["x"])[None, None, :]
    src = (
        ((lax.axis_index("z") - dz) % sizes["z"]) * (sizes["y"] * sizes["x"])
        + ((lax.axis_index("y") - dy) % sizes["y"]) * sizes["x"]
        + (lax.axis_index("x") - dx) % sizes["x"]
    ).reshape(-1)
    chip_ctx = lax.all_gather(token_ctx, "rep", axis=0, tiled=True)
    chip_ctx = chip_ctx.reshape(chip_ctx.shape[0], -1, feat_block)
    chip_ctx = jnp.take(chip_ctx, src, axis=1).reshape(chip_ctx.shape[0], -1)
    att_cols = jnp.dot(chip_ctx, proj_rows, preferred_element_type=jnp.float32)
    att_cols = att_cols.reshape(rep_count, tokens, half)
    attention = lax.all_to_all(att_cols, "rep", split_axis=0, concat_axis=2, tiled=True)
    attention = attention.reshape(tokens, model_width)

    hidden = (resid_in.astype(jnp.float32) + attention).astype(jnp.bfloat16)
    normed = rms_norm(hidden, norm_gain)
    logits = jnp.dot(normed, router, preferred_element_type=jnp.float32)
    experts = router.shape[1]
    picked_mask = (
        routes[:, :, None] == jnp.arange(experts, dtype=jnp.int32)[None, None, :]
    ).astype(jnp.int32)
    picked = jnp.sum(picked_mask.astype(jnp.float32) * logits[:, None, :], axis=2)
    raised = jnp.exp(picked)
    route_weight = (raised / jnp.sum(raised, axis=1, keepdims=True)).astype(jnp.bfloat16)

    named_count = jnp.sum(picked_mask, axis=1)
    before = jnp.cumsum(named_count, axis=0) - named_count
    order_rank = jnp.sum(picked_mask * before[:, None, :], axis=2)
    groups = experts // rep_count
    slot_index = ((routes % groups) * rep_count + routes // groups) * MOST + order_rank
    slot_total = experts * MOST
    slot_hits = slot_index[None] == jnp.arange(slot_total, dtype=jnp.int32)[:, None, None]
    placing = jnp.any(slot_hits, axis=2).astype(jnp.bfloat16)
    outgoing = jnp.dot(placing, normed, preferred_element_type=jnp.bfloat16)
    outgoing = outgoing.reshape(groups, rep_count, MOST, model_width)
    arrived = lax.all_to_all(outgoing, "rep", split_axis=1, concat_axis=1, tiled=True)
    arrived = lax.all_to_all(arrived, ("z", "y"), split_axis=0, concat_axis=0, tiled=True)
    rows = arrived.reshape(-1, model_width)

    block_size = w_gate.shape[1]
    quarters = sizes["x"]
    gate_h = jnp.dot(rows, gate_all, preferred_element_type=jnp.float32)
    up_h = jnp.dot(rows, up_all, preferred_element_type=jnp.float32)
    activated = (jax.nn.silu(gate_h) * up_h).astype(jnp.bfloat16)
    activated = activated.reshape(-1, quarters, block_size)
    produced = jnp.einsum(
        "sqj,qjd->sqd",
        activated,
        down_all.reshape(quarters, block_size, model_width),
        preferred_element_type=jnp.float32,
    ).astype(jnp.bfloat16)
    summed = jnp.sum(produced.astype(jnp.float32), axis=1).astype(jnp.bfloat16)
    summed = summed.reshape(arrived.shape)
    back = lax.all_to_all(summed, ("z", "y"), split_axis=0, concat_axis=0, tiled=True)
    returned = lax.all_to_all(back, "rep", split_axis=1, concat_axis=1, tiled=True)
    returned = returned.reshape(slot_total, model_width)

    weighing = jnp.sum(
        slot_hits.astype(jnp.float32) * route_weight.astype(jnp.float32)[None], axis=2
    ).T.astype(jnp.bfloat16)
    expert_sum = jnp.dot(weighing, returned, preferred_element_type=jnp.float32)
    resid_out = (hidden.astype(jnp.float32) + expert_sum).astype(jnp.bfloat16)
    next_normed = rms_norm(resid_out, next_gain)
    return (resid_out, next_normed)


def solution(mesh):
    rep_count = mesh.shape["rep"]
    ep_count = mesh.shape["ep"]
    units = 65536 // (rep_count * ep_count)
    owners = max(FF_E // units, 1)
    rows_of = 4 if (ep_count // owners) % 4 == 0 else 1
    devices = mesh.devices.reshape(rep_count, ep_count // owners // rows_of, rows_of, owners)
    grid = Mesh(devices, ("rep", "z", "y", "x"))
    tok = ("rep", "z", "y", "x")
    feat = ("z", "y", "x")
    in_specs = (
        P(tok, None),
        P("rep", feat),
        P(feat, None),
        P(),
        P(),
        P(tok, None),
        P(None, tok),
        P(None, tok),
        P(tok, None),
        P(),
    )
    out_specs = (P(tok, None), P(tok, None))
    return jax.shard_map(body, mesh=grid, in_specs=in_specs, out_specs=out_specs, check_vma=False)
```

```python
import jax
import jax.numpy as jnp
from jax import lax
from jax.sharding import Mesh
from jax.sharding import PartitionSpec as P

FF_E = 1024
MOST = 10


def rms_norm(values, gain_row):
    widened = values.astype(jnp.float32)
    factor = lax.rsqrt(jnp.mean(widened * widened, axis=-1, keepdims=True) + 1e-06)
    return (widened * factor * gain_row).astype(jnp.bfloat16)


def shift_pairs(size, offset):
    return [(i, (i + offset) % size) for i in range(size)]


def gather_proj(block, sizes):
    x_n, z_n, y_n = sizes["x"], sizes["z"], sizes["y"]
    parts = [block] + [lax.ppermute(block, "x", shift_pairs(x_n, d)) for d in range(1, x_n)]
    block = jnp.stack(parts)
    parts = [block] + [lax.ppermute(block, "z", shift_pairs(z_n, d)) for d in range(1, z_n)]
    block = jnp.stack(parts)
    if y_n == 4:
        ahead = lax.ppermute(block, "y", shift_pairs(4, 1))
        behind = lax.ppermute(block, "y", shift_pairs(4, 3))
        cut = block.shape[0] // 2
        far_a = lax.ppermute(ahead[:cut], "y", shift_pairs(4, 1))
        far_b = lax.ppermute(behind[cut:], "y", shift_pairs(4, 3))
        parts = [block, ahead, jnp.concatenate([far_a, far_b]), behind]
    else:
        parts = [block] + [lax.ppermute(block, "y", shift_pairs(y_n, d)) for d in range(1, y_n)]
    return jnp.stack(parts)


def body(resid_in, context, out_proj, norm_gain, router, routes, w_gate, w_up, w_down, next_gain):
    model_width = resid_in.shape[1]
    tokens = resid_in.shape[0]
    sizes = {a: lax.axis_size(a) for a in ("rep", "z", "y", "x")}
    rep_count = sizes["rep"]
    rep_id = lax.axis_index("rep")
    chip = ("z", "y", "x")

    gate_all = lax.all_gather(w_gate, "x", axis=1, tiled=True)
    up_all = lax.all_gather(w_up, "x", axis=1, tiled=True)
    down_all = lax.all_gather(w_down, "x", axis=0, tiled=True)

    token_ctx = lax.all_to_all(context, chip, split_axis=0, concat_axis=1, tiled=True)
    half = model_width // rep_count
    proj_half = lax.dynamic_slice_in_dim(out_proj, rep_id * half, half, axis=1)
    proj_rows = gather_proj(proj_half, sizes)
    feat_block = proj_half.shape[0]
    proj_rows = proj_rows.reshape(-1, half)
    dy = jnp.arange(sizes["y"])[:, None, None]
    dz = jnp.arange(sizes["z"])[None, :, None]
    dx = jnp.arange(sizes["x"])[None, None, :]
    src = (
        ((lax.axis_index("z") - dz) % sizes["z"]) * (sizes["y"] * sizes["x"])
        + ((lax.axis_index("y") - dy) % sizes["y"]) * sizes["x"]
        + (lax.axis_index("x") - dx) % sizes["x"]
    ).reshape(-1)
    chip_ctx = lax.all_gather(token_ctx, "rep", axis=0, tiled=True)
    chip_ctx = chip_ctx.reshape(chip_ctx.shape[0], -1, feat_block)
    chip_ctx = jnp.take(chip_ctx, src, axis=1).reshape(chip_ctx.shape[0], -1)
    att_cols = jnp.dot(chip_ctx, proj_rows, preferred_element_type=jnp.float32)
    att_cols = att_cols.reshape(rep_count, tokens, half)
    attention = lax.all_to_all(att_cols, "rep", split_axis=0, concat_axis=2, tiled=True)
    attention = attention.reshape(tokens, model_width)

    hidden = (resid_in.astype(jnp.float32) + attention).astype(jnp.bfloat16)
    normed = rms_norm(hidden, norm_gain)
    logits = jnp.dot(normed, router, preferred_element_type=jnp.float32)
    experts = router.shape[1]
    picked_mask = (
        routes[:, :, None] == jnp.arange(experts, dtype=jnp.int32)[None, None, :]
    ).astype(jnp.int32)
    picked = jnp.sum(picked_mask.astype(jnp.float32) * logits[:, None, :], axis=2)
    raised = jnp.exp(picked)
    route_weight = (raised / jnp.sum(raised, axis=1, keepdims=True)).astype(jnp.bfloat16)

    named_count = jnp.sum(picked_mask, axis=1)
    before = jnp.cumsum(named_count, axis=0) - named_count
    order_rank = jnp.sum(picked_mask * before[:, None, :], axis=2)
    groups = experts // rep_count
    slot_index = ((routes % groups) * rep_count + routes // groups) * MOST + order_rank
    chip_slot = lax.all_gather(slot_index, "rep", axis=0, tiled=True)
    chip_weight = lax.all_gather(route_weight, "rep", axis=0, tiled=True)
    chip_normed = lax.all_gather(normed, "rep", axis=0, tiled=True)
    source_core = (jnp.arange(chip_slot.shape[0], dtype=jnp.int32) // tokens)[:, None]
    group_of = chip_slot // (rep_count * MOST)
    core_of = (chip_slot // MOST) % rep_count
    rank_of = chip_slot % MOST
    local_slot = jnp.where(
        core_of == rep_id, (group_of * rep_count + source_core) * MOST + rank_of, -1
    )
    slot_total = groups * rep_count * MOST
    slot_hits = local_slot[None] == jnp.arange(slot_total, dtype=jnp.int32)[:, None, None]
    placing = jnp.any(slot_hits, axis=2).astype(jnp.bfloat16)
    outgoing = jnp.dot(placing, chip_normed, preferred_element_type=jnp.bfloat16)
    outgoing = outgoing.reshape(groups, rep_count, MOST, model_width)
    arrived = lax.all_to_all(outgoing, ("z", "y"), split_axis=0, concat_axis=0, tiled=True)
    rows = arrived.reshape(-1, model_width)

    block_size = w_gate.shape[1]
    quarters = sizes["x"]
    gate_h = jnp.dot(rows, gate_all, preferred_element_type=jnp.float32)
    up_h = jnp.dot(rows, up_all, preferred_element_type=jnp.float32)
    activated = (jax.nn.silu(gate_h) * up_h).astype(jnp.bfloat16)
    activated = activated.reshape(-1, quarters, block_size)
    produced = jnp.einsum(
        "sqj,qjd->sqd",
        activated,
        down_all.reshape(quarters, block_size, model_width),
        preferred_element_type=jnp.float32,
    ).astype(jnp.bfloat16)
    summed = jnp.sum(produced.astype(jnp.float32), axis=1).astype(jnp.bfloat16)
    summed = summed.reshape(arrived.shape)
    back = lax.all_to_all(summed, ("z", "y"), split_axis=0, concat_axis=0, tiled=True)
    back = back.reshape(slot_total, model_width)

    weighing = jnp.sum(
        slot_hits.astype(jnp.float32) * chip_weight.astype(jnp.float32)[None], axis=2
    ).T.astype(jnp.bfloat16)
    partial = jnp.dot(weighing, back, preferred_element_type=jnp.float32)
    partial = partial.reshape(rep_count, tokens, model_width)
    partial = lax.all_to_all(partial, "rep", split_axis=0, concat_axis=0, tiled=True)
    expert_sum = jnp.sum(partial, axis=0)
    resid_out = (hidden.astype(jnp.float32) + expert_sum).astype(jnp.bfloat16)
    next_normed = rms_norm(resid_out, next_gain)
    return (resid_out, next_normed)


def solution(mesh):
    rep_count = mesh.shape["rep"]
    ep_count = mesh.shape["ep"]
    units = 65536 // (rep_count * ep_count)
    owners = max(FF_E // units, 1)
    rows_of = 4 if (ep_count // owners) % 4 == 0 else 1
    devices = mesh.devices.reshape(rep_count, ep_count // owners // rows_of, rows_of, owners)
    grid = Mesh(devices, ("rep", "z", "y", "x"))
    tok = ("rep", "z", "y", "x")
    feat = ("z", "y", "x")
    in_specs = (
        P(tok, None),
        P("rep", feat),
        P(feat, None),
        P(),
        P(),
        P(tok, None),
        P(None, tok),
        P(None, tok),
        P(tok, None),
        P(),
    )
    out_specs = (P(tok, None), P(tok, None))
    return jax.shard_map(body, mesh=grid, in_specs=in_specs, out_specs=out_specs, check_vma=False)
```

```python
import jax
import jax.numpy as jnp
from jax import lax
from jax.sharding import Mesh
from jax.sharding import PartitionSpec as P

FF_E = 1024
MOST = 10


def rms_norm(values, gain_row):
    widened = values.astype(jnp.float32)
    factor = lax.rsqrt(jnp.mean(widened * widened, axis=-1, keepdims=True) + 1e-06)
    return (widened * factor * gain_row).astype(jnp.bfloat16)


def shift_pairs(size, offset):
    return [(i, (i + offset) % size) for i in range(size)]


def gather_proj(block, sizes):
    x_n, z_n, y_n = sizes["x"], sizes["z"], sizes["y"]
    parts = [block] + [lax.ppermute(block, "x", shift_pairs(x_n, d)) for d in range(1, x_n)]
    block = jnp.stack(parts)
    parts = [block] + [lax.ppermute(block, "z", shift_pairs(z_n, d)) for d in range(1, z_n)]
    block = jnp.stack(parts)
    if y_n == 4:
        ahead = lax.ppermute(block, "y", shift_pairs(4, 1))
        behind = lax.ppermute(block, "y", shift_pairs(4, 3))
        cut = block.shape[0] // 2
        far_a = lax.ppermute(ahead[:cut], "y", shift_pairs(4, 1))
        far_b = lax.ppermute(behind[cut:], "y", shift_pairs(4, 3))
        parts = [block, ahead, jnp.concatenate([far_a, far_b]), behind]
    else:
        parts = [block] + [lax.ppermute(block, "y", shift_pairs(y_n, d)) for d in range(1, y_n)]
    return jnp.stack(parts)


def body(resid_in, context, out_proj, norm_gain, router, routes, w_gate, w_up, w_down, next_gain):
    model_width = resid_in.shape[1]
    tokens = resid_in.shape[0]
    sizes = {a: lax.axis_size(a) for a in ("rep", "z", "y", "x")}
    rep_count = sizes["rep"]
    rep_id = lax.axis_index("rep")
    chip = ("z", "y", "x")

    gate_all = lax.all_gather(w_gate, "x", axis=1, tiled=True)
    up_all = lax.all_gather(w_up, "x", axis=1, tiled=True)
    down_all = lax.all_gather(w_down, "x", axis=0, tiled=True)

    token_ctx = lax.all_to_all(context, chip, split_axis=0, concat_axis=1, tiled=True)
    half = model_width // rep_count
    proj_half = lax.dynamic_slice_in_dim(out_proj, rep_id * half, half, axis=1)
    proj_rows = gather_proj(proj_half, sizes)
    feat_block = proj_half.shape[0]
    proj_rows = proj_rows.reshape(-1, half)
    dy = jnp.arange(sizes["y"])[:, None, None]
    dz = jnp.arange(sizes["z"])[None, :, None]
    dx = jnp.arange(sizes["x"])[None, None, :]
    src = (
        ((lax.axis_index("z") - dz) % sizes["z"]) * (sizes["y"] * sizes["x"])
        + ((lax.axis_index("y") - dy) % sizes["y"]) * sizes["x"]
        + (lax.axis_index("x") - dx) % sizes["x"]
    ).reshape(-1)
    chip_ctx = lax.all_gather(token_ctx, "rep", axis=0, tiled=True)
    chip_ctx = chip_ctx.reshape(chip_ctx.shape[0], -1, feat_block)
    chip_ctx = jnp.take(chip_ctx, src, axis=1).reshape(chip_ctx.shape[0], -1)
    att_cols = jnp.dot(chip_ctx, proj_rows, preferred_element_type=jnp.float32)
    att_cols = att_cols.reshape(rep_count, tokens, half)
    attention = lax.all_to_all(att_cols, "rep", split_axis=0, concat_axis=2, tiled=True)
    attention = attention.reshape(tokens, model_width)

    hidden = (resid_in.astype(jnp.float32) + attention).astype(jnp.bfloat16)
    normed = rms_norm(hidden, norm_gain)
    logits = jnp.dot(normed, router, preferred_element_type=jnp.float32)
    experts = router.shape[1]
    picked_mask = (
        routes[:, :, None] == jnp.arange(experts, dtype=jnp.int32)[None, None, :]
    ).astype(jnp.int32)
    picked = jnp.sum(picked_mask.astype(jnp.float32) * logits[:, None, :], axis=2)
    raised = jnp.exp(picked)
    route_weight = (raised / jnp.sum(raised, axis=1, keepdims=True)).astype(jnp.bfloat16)

    named_count = jnp.sum(picked_mask, axis=1)
    before = jnp.cumsum(named_count, axis=0) - named_count
    order_rank = jnp.sum(picked_mask * before[:, None, :], axis=2)
    groups = experts // rep_count
    slot_index = ((routes % groups) * rep_count + routes // groups) * MOST + order_rank
    chip_slot = lax.all_gather(slot_index, "rep", axis=0, tiled=True)
    chip_weight = lax.all_gather(route_weight, "rep", axis=0, tiled=True)
    chip_normed = lax.all_gather(normed, "rep", axis=0, tiled=True)
    source_core = (jnp.arange(chip_slot.shape[0], dtype=jnp.int32) // tokens)[:, None]
    group_of = chip_slot // (rep_count * MOST)
    core_of = (chip_slot // MOST) % rep_count
    rank_of = chip_slot % MOST
    local_slot = jnp.where(
        core_of == rep_id, (group_of * rep_count + source_core) * MOST + rank_of, -1
    )
    slot_total = groups * rep_count * MOST
    slot_hits = local_slot[None] == jnp.arange(slot_total, dtype=jnp.int32)[:, None, None]
    placing = jnp.any(slot_hits, axis=2).astype(jnp.bfloat16)
    outgoing = jnp.dot(placing, chip_normed, preferred_element_type=jnp.bfloat16)
    arrived = lax.all_to_all(outgoing, ("z", "y"), split_axis=0, concat_axis=0, tiled=True)
    rows = arrived.reshape(-1, model_width)

    block_size = w_gate.shape[1]
    quarters = sizes["x"]
    gate_h = jnp.dot(rows, gate_all, preferred_element_type=jnp.float32)
    up_h = jnp.dot(rows, up_all, preferred_element_type=jnp.float32)
    activated = (jax.nn.silu(gate_h) * up_h).astype(jnp.bfloat16)
    activated = activated.reshape(-1, quarters, block_size)
    produced = jnp.einsum(
        "sqj,qjd->sqd",
        activated,
        down_all.reshape(quarters, block_size, model_width),
        preferred_element_type=jnp.float32,
    ).astype(jnp.bfloat16)
    summed = jnp.sum(produced.astype(jnp.float32), axis=1).astype(jnp.bfloat16)
    back = lax.all_to_all(summed, ("z", "y"), split_axis=0, concat_axis=0, tiled=True)
    back = back.reshape(slot_total, model_width)

    weighing = jnp.sum(
        slot_hits.astype(jnp.float32) * chip_weight.astype(jnp.float32)[None], axis=2
    ).T.astype(jnp.bfloat16)
    partial = jnp.dot(weighing, back, preferred_element_type=jnp.float32)
    partial = partial.reshape(rep_count, tokens, model_width)
    partial = lax.all_to_all(partial, "rep", split_axis=0, concat_axis=0, tiled=True)
    expert_sum = jnp.sum(partial, axis=0)
    resid_out = (hidden.astype(jnp.float32) + expert_sum).astype(jnp.bfloat16)
    next_normed = rms_norm(resid_out, next_gain)
    return (resid_out, next_normed)


def solution(mesh):
    rep_count = mesh.shape["rep"]
    ep_count = mesh.shape["ep"]
    units = 65536 // (rep_count * ep_count)
    owners = max(FF_E // units, 1)
    rows_of = 4 if (ep_count // owners) % 4 == 0 else 1
    devices = mesh.devices.reshape(rep_count, ep_count // owners // rows_of, rows_of, owners)
    grid = Mesh(devices, ("rep", "z", "y", "x"))
    tok = ("rep", "z", "y", "x")
    feat = ("z", "y", "x")
    in_specs = (
        P(tok, None),
        P("rep", feat),
        P(feat, None),
        P(),
        P(),
        P(tok, None),
        P(None, tok),
        P(None, tok),
        P(tok, None),
        P(),
    )
    out_specs = (P(tok, None), P(tok, None))
    return jax.shard_map(body, mesh=grid, in_specs=in_specs, out_specs=out_specs, check_vma=False)
```

```python
import jax
import jax.numpy as jnp
from jax import lax
from jax.sharding import Mesh
from jax.sharding import PartitionSpec as P

FF_E = 1024
MOST = 10


def rms_norm(values, gain_row):
    widened = values.astype(jnp.float32)
    factor = lax.rsqrt(jnp.mean(widened * widened, axis=-1, keepdims=True) + 1e-06)
    return (widened * factor * gain_row).astype(jnp.bfloat16)


def shift_pairs(size, offset):
    return [(i, (i + offset) % size) for i in range(size)]


def gather_proj(block, sizes):
    x_n, z_n, y_n = sizes["x"], sizes["z"], sizes["y"]
    parts = [block] + [lax.ppermute(block, "x", shift_pairs(x_n, d)) for d in range(1, x_n)]
    block = jnp.stack(parts)
    parts = [block] + [lax.ppermute(block, "z", shift_pairs(z_n, d)) for d in range(1, z_n)]
    block = jnp.stack(parts)
    if y_n == 4:
        ahead = lax.ppermute(block, "y", shift_pairs(4, 1))
        behind = lax.ppermute(block, "y", shift_pairs(4, 3))
        cut = block.shape[0] // 2
        far_a = lax.ppermute(ahead[:cut], "y", shift_pairs(4, 1))
        far_b = lax.ppermute(behind[cut:], "y", shift_pairs(4, 3))
        parts = [block, ahead, jnp.concatenate([far_a, far_b]), behind]
    else:
        parts = [block] + [lax.ppermute(block, "y", shift_pairs(y_n, d)) for d in range(1, y_n)]
    return jnp.stack(parts)


def body(resid_in, context, out_proj, norm_gain, router, routes, w_gate, w_up, w_down, next_gain):
    model_width = resid_in.shape[1]
    tokens = resid_in.shape[0]
    sizes = {a: lax.axis_size(a) for a in ("rep", "z", "y", "x")}
    rep_count = sizes["rep"]
    rep_id = lax.axis_index("rep")
    chip = ("z", "y", "x")

    gate_all = lax.all_gather(w_gate, "x", axis=1, tiled=True)
    up_all = lax.all_gather(w_up, "x", axis=1, tiled=True)
    down_all = lax.all_gather(w_down, "x", axis=0, tiled=True)

    token_ctx = lax.all_to_all(context, chip, split_axis=0, concat_axis=1, tiled=True)
    half = model_width // rep_count
    proj_half = lax.dynamic_slice_in_dim(out_proj, rep_id * half, half, axis=1)
    proj_rows = gather_proj(proj_half, sizes)
    feat_block = proj_half.shape[0]
    proj_rows = proj_rows.reshape(-1, half)
    dy = jnp.arange(sizes["y"])[:, None, None]
    dz = jnp.arange(sizes["z"])[None, :, None]
    dx = jnp.arange(sizes["x"])[None, None, :]
    src = (
        ((lax.axis_index("z") - dz) % sizes["z"]) * (sizes["y"] * sizes["x"])
        + ((lax.axis_index("y") - dy) % sizes["y"]) * sizes["x"]
        + (lax.axis_index("x") - dx) % sizes["x"]
    ).reshape(-1)
    chip_ctx = lax.all_gather(token_ctx, "rep", axis=0, tiled=True)
    chip_ctx = chip_ctx.reshape(chip_ctx.shape[0], -1, feat_block)
    chip_ctx = jnp.take(chip_ctx, src, axis=1).reshape(chip_ctx.shape[0], -1)
    att_cols = jnp.dot(chip_ctx, proj_rows, preferred_element_type=jnp.float32)
    att_cols = att_cols.reshape(rep_count, tokens, half)
    attention = lax.all_to_all(att_cols, "rep", split_axis=0, concat_axis=2, tiled=True)
    attention = attention.reshape(tokens, model_width)

    hidden = (resid_in.astype(jnp.float32) + attention).astype(jnp.bfloat16)
    normed = rms_norm(hidden, norm_gain)
    logits = jnp.dot(normed, router, preferred_element_type=jnp.float32)
    experts = router.shape[1]
    picked_mask = (
        routes[:, :, None] == jnp.arange(experts, dtype=jnp.int32)[None, None, :]
    ).astype(jnp.int32)
    picked = jnp.sum(picked_mask.astype(jnp.float32) * logits[:, None, :], axis=2)
    raised = jnp.exp(picked)
    route_weight = (raised / jnp.sum(raised, axis=1, keepdims=True)).astype(jnp.bfloat16)

    named_count = jnp.sum(picked_mask, axis=1)
    before = jnp.cumsum(named_count, axis=0) - named_count
    order_rank = jnp.sum(picked_mask * before[:, None, :], axis=2)
    groups = experts // rep_count
    slot_index = ((routes % groups) * rep_count + routes // groups) * MOST + order_rank
    chip_slot = lax.all_gather(slot_index, "rep", axis=0, tiled=True)
    chip_weight = lax.all_gather(route_weight, "rep", axis=0, tiled=True)
    chip_normed = lax.all_gather(normed, "rep", axis=0, tiled=True)
    source_core = (jnp.arange(chip_slot.shape[0], dtype=jnp.int32) // tokens)[:, None]
    group_of = chip_slot // (rep_count * MOST)
    core_of = (chip_slot // MOST) % rep_count
    rank_of = chip_slot % MOST
    local_slot = jnp.where(
        core_of == rep_id, (group_of * MOST + rank_of) * rep_count + source_core, -1
    )
    slot_total = groups * rep_count * MOST
    slot_hits = local_slot[None] == jnp.arange(slot_total, dtype=jnp.int32)[:, None, None]
    placing = jnp.any(slot_hits, axis=2).astype(jnp.bfloat16)
    outgoing = jnp.dot(placing, chip_normed, preferred_element_type=jnp.bfloat16)
    outgoing = outgoing.reshape(groups, MOST, rep_count, model_width)
    arrived = lax.all_to_all(outgoing, ("z", "y"), split_axis=0, concat_axis=0, tiled=True)
    rows = arrived.reshape(-1, model_width)

    block_size = w_gate.shape[1]
    quarters = sizes["x"]
    gate_h = jnp.dot(rows, gate_all, preferred_element_type=jnp.float32)
    up_h = jnp.dot(rows, up_all, preferred_element_type=jnp.float32)
    activated = (jax.nn.silu(gate_h) * up_h).astype(jnp.bfloat16)
    activated = activated.reshape(-1, quarters, block_size)
    produced = jnp.einsum(
        "sqj,qjd->sqd",
        activated,
        down_all.reshape(quarters, block_size, model_width),
        preferred_element_type=jnp.float32,
    ).astype(jnp.bfloat16)
    summed = jnp.sum(produced.astype(jnp.float32), axis=1).astype(jnp.bfloat16)
    summed = summed.reshape(arrived.shape)
    back = lax.all_to_all(summed, ("z", "y"), split_axis=0, concat_axis=0, tiled=True)
    back = back.reshape(slot_total, model_width)

    weighing = jnp.sum(
        slot_hits.astype(jnp.float32) * chip_weight.astype(jnp.float32)[None], axis=2
    ).T.astype(jnp.bfloat16)
    partial = jnp.dot(weighing, back, preferred_element_type=jnp.float32)
    partial = partial.reshape(rep_count, tokens, model_width)
    partial = lax.all_to_all(partial, "rep", split_axis=0, concat_axis=0, tiled=True)
    expert_sum = jnp.sum(partial, axis=0)
    resid_out = (hidden.astype(jnp.float32) + expert_sum).astype(jnp.bfloat16)
    next_normed = rms_norm(resid_out, next_gain)
    return (resid_out, next_normed)


def solution(mesh):
    rep_count = mesh.shape["rep"]
    ep_count = mesh.shape["ep"]
    units = 65536 // (rep_count * ep_count)
    owners = max(FF_E // units, 1)
    rows_of = 4 if (ep_count // owners) % 4 == 0 else 1
    devices = mesh.devices.reshape(rep_count, ep_count // owners // rows_of, rows_of, owners)
    grid = Mesh(devices, ("rep", "z", "y", "x"))
    tok = ("rep", "z", "y", "x")
    feat = ("z", "y", "x")
    in_specs = (
        P(tok, None),
        P("rep", feat),
        P(feat, None),
        P(),
        P(),
        P(tok, None),
        P(None, tok),
        P(None, tok),
        P(tok, None),
        P(),
    )
    out_specs = (P(tok, None), P(tok, None))
    return jax.shard_map(body, mesh=grid, in_specs=in_specs, out_specs=out_specs, check_vma=False)
```

```python
import jax
import jax.numpy as jnp
from jax import lax
from jax.sharding import Mesh
from jax.sharding import PartitionSpec as P

FF_E = 1024
MOST = 10


def rms_norm(values, gain_row):
    widened = values.astype(jnp.float32)
    factor = lax.rsqrt(jnp.mean(widened * widened, axis=-1, keepdims=True) + 1e-06)
    return (widened * factor * gain_row).astype(jnp.bfloat16)


def shift_pairs(size, offset):
    return [(i, (i + offset) % size) for i in range(size)]


def gather_proj(block, sizes):
    x_n, z_n, y_n = sizes["x"], sizes["z"], sizes["y"]
    parts = [block] + [lax.ppermute(block, "x", shift_pairs(x_n, d)) for d in range(1, x_n)]
    block = jnp.stack(parts)
    parts = [block] + [lax.ppermute(block, "z", shift_pairs(z_n, d)) for d in range(1, z_n)]
    block = jnp.stack(parts)
    if y_n == 4:
        ahead = lax.ppermute(block, "y", shift_pairs(4, 1))
        behind = lax.ppermute(block, "y", shift_pairs(4, 3))
        cut = block.shape[0] // 2
        far_a = lax.ppermute(ahead[:cut], "y", shift_pairs(4, 1))
        far_b = lax.ppermute(behind[cut:], "y", shift_pairs(4, 3))
        parts = [block, ahead, jnp.concatenate([far_a, far_b]), behind]
    else:
        parts = [block] + [lax.ppermute(block, "y", shift_pairs(y_n, d)) for d in range(1, y_n)]
    return jnp.stack(parts)


def body(resid_in, context, out_proj, norm_gain, router, routes, w_gate, w_up, w_down, next_gain):
    model_width = resid_in.shape[1]
    tokens = resid_in.shape[0]
    sizes = {a: lax.axis_size(a) for a in ("rep", "z", "y", "x")}
    rep_count = sizes["rep"]
    rep_id = lax.axis_index("rep")
    chip = ("z", "y", "x")

    gate_all = lax.all_gather(w_gate, "x", axis=1, tiled=True)
    up_all = lax.all_gather(w_up, "x", axis=1, tiled=True)
    down_all = lax.all_gather(w_down, "x", axis=0, tiled=True)

    token_ctx = lax.all_to_all(context, chip, split_axis=0, concat_axis=1, tiled=True)
    half = model_width // rep_count
    proj_half = lax.dynamic_slice_in_dim(out_proj, rep_id * half, half, axis=1)
    proj_rows = gather_proj(proj_half, sizes)
    feat_block = proj_half.shape[0]
    proj_rows = proj_rows.reshape(-1, half)
    dy = jnp.arange(sizes["y"])[:, None, None]
    dz = jnp.arange(sizes["z"])[None, :, None]
    dx = jnp.arange(sizes["x"])[None, None, :]
    src = (
        ((lax.axis_index("z") - dz) % sizes["z"]) * (sizes["y"] * sizes["x"])
        + ((lax.axis_index("y") - dy) % sizes["y"]) * sizes["x"]
        + (lax.axis_index("x") - dx) % sizes["x"]
    ).reshape(-1)
    chip_ctx = lax.all_gather(token_ctx, "rep", axis=0, tiled=True)
    chip_ctx = chip_ctx.reshape(chip_ctx.shape[0], -1, feat_block)
    chip_ctx = jnp.take(chip_ctx, src, axis=1).reshape(chip_ctx.shape[0], -1)
    att_cols = jnp.dot(chip_ctx, proj_rows, preferred_element_type=jnp.float32)
    att_full = lax.all_gather(att_cols, "rep", axis=1, tiled=True)
    chip_resid = lax.all_gather(resid_in, "rep", axis=0, tiled=True)
    chip_routes = lax.all_gather(routes, "rep", axis=0, tiled=True)
    chip_hidden = (chip_resid.astype(jnp.float32) + att_full).astype(jnp.bfloat16)
    hidden = lax.dynamic_slice_in_dim(chip_hidden, rep_id * tokens, tokens, axis=0)
    chip_normed = rms_norm(chip_hidden, norm_gain)
    logits = jnp.dot(chip_normed, router, preferred_element_type=jnp.float32)
    experts = router.shape[1]
    picked_mask = (
        chip_routes[:, :, None] == jnp.arange(experts, dtype=jnp.int32)[None, None, :]
    ).astype(jnp.int32)
    picked = jnp.sum(picked_mask.astype(jnp.float32) * logits[:, None, :], axis=2)
    raised = jnp.exp(picked)
    chip_weight = (raised / jnp.sum(raised, axis=1, keepdims=True)).astype(jnp.bfloat16)

    named_count = jnp.sum(picked_mask, axis=1).reshape(rep_count, tokens, experts)
    before = (jnp.cumsum(named_count, axis=1) - named_count).reshape(rep_count * tokens, experts)
    rank_of = jnp.sum(picked_mask * before[:, None, :], axis=2)
    groups = experts // rep_count
    source_core = (jnp.arange(chip_routes.shape[0], dtype=jnp.int32) // tokens)[:, None]
    local_slot = jnp.where(
        chip_routes // groups == rep_id,
        ((chip_routes % groups) * MOST + rank_of) * rep_count + source_core,
        -1,
    )
    slot_total = groups * rep_count * MOST
    slot_hits = local_slot[None] == jnp.arange(slot_total, dtype=jnp.int32)[:, None, None]
    placing = jnp.any(slot_hits, axis=2).astype(jnp.bfloat16)
    outgoing = jnp.dot(placing, chip_normed, preferred_element_type=jnp.bfloat16)
    outgoing = outgoing.reshape(groups, MOST, rep_count, model_width)
    arrived = lax.all_to_all(outgoing, ("z", "y"), split_axis=0, concat_axis=0, tiled=True)
    rows = arrived.reshape(-1, model_width)

    block_size = w_gate.shape[1]
    quarters = sizes["x"]
    gate_h = jnp.dot(rows, gate_all, preferred_element_type=jnp.float32)
    up_h = jnp.dot(rows, up_all, preferred_element_type=jnp.float32)
    activated = (jax.nn.silu(gate_h) * up_h).astype(jnp.bfloat16)
    activated = activated.reshape(-1, quarters, block_size)
    produced = jnp.einsum(
        "sqj,qjd->sqd",
        activated,
        down_all.reshape(quarters, block_size, model_width),
        preferred_element_type=jnp.float32,
    ).astype(jnp.bfloat16)
    summed = jnp.sum(produced.astype(jnp.float32), axis=1).astype(jnp.bfloat16)
    summed = summed.reshape(arrived.shape)
    back = lax.all_to_all(summed, ("z", "y"), split_axis=0, concat_axis=0, tiled=True)
    back = back.reshape(slot_total, model_width)

    weighing = jnp.sum(
        slot_hits.astype(jnp.float32) * chip_weight.astype(jnp.float32)[None], axis=2
    ).T.astype(jnp.bfloat16)
    partial = jnp.dot(weighing, back, preferred_element_type=jnp.float32)
    partial = partial.reshape(rep_count, tokens, model_width)
    partial = lax.all_to_all(partial, "rep", split_axis=0, concat_axis=0, tiled=True)
    expert_sum = jnp.sum(partial, axis=0)
    resid_out = (hidden.astype(jnp.float32) + expert_sum).astype(jnp.bfloat16)
    next_normed = rms_norm(resid_out, next_gain)
    return (resid_out, next_normed)


def solution(mesh):
    rep_count = mesh.shape["rep"]
    ep_count = mesh.shape["ep"]
    units = 65536 // (rep_count * ep_count)
    owners = max(FF_E // units, 1)
    rows_of = 4 if (ep_count // owners) % 4 == 0 else 1
    devices = mesh.devices.reshape(rep_count, ep_count // owners // rows_of, rows_of, owners)
    grid = Mesh(devices, ("rep", "z", "y", "x"))
    tok = ("rep", "z", "y", "x")
    feat = ("z", "y", "x")
    in_specs = (
        P(tok, None),
        P("rep", feat),
        P(feat, None),
        P(),
        P(),
        P(tok, None),
        P(None, tok),
        P(None, tok),
        P(tok, None),
        P(),
    )
    out_specs = (P(tok, None), P(tok, None))
    return jax.shard_map(body, mesh=grid, in_specs=in_specs, out_specs=out_specs, check_vma=False)
```

```python
import jax
import jax.numpy as jnp
from jax import lax
from jax.sharding import Mesh
from jax.sharding import PartitionSpec as P

FF_E = 1024
MOST = 10


def rms_norm(values, gain_row):
    widened = values.astype(jnp.float32)
    factor = lax.rsqrt(jnp.mean(widened * widened, axis=-1, keepdims=True) + 1e-06)
    return (widened * factor * gain_row).astype(jnp.bfloat16)


def shift_pairs(size, offset):
    return [(i, (i + offset) % size) for i in range(size)]


def gather_proj(block, sizes):
    x_n, z_n, y_n = sizes["x"], sizes["z"], sizes["y"]
    parts = [block] + [lax.ppermute(block, "x", shift_pairs(x_n, d)) for d in range(1, x_n)]
    block = jnp.stack(parts)
    parts = [block] + [lax.ppermute(block, "z", shift_pairs(z_n, d)) for d in range(1, z_n)]
    block = jnp.stack(parts)
    if y_n == 4:
        ahead = lax.ppermute(block, "y", shift_pairs(4, 1))
        behind = lax.ppermute(block, "y", shift_pairs(4, 3))
        cut = block.shape[0] // 2
        far_a = lax.ppermute(ahead[:cut], "y", shift_pairs(4, 1))
        far_b = lax.ppermute(behind[cut:], "y", shift_pairs(4, 3))
        parts = [block, ahead, jnp.concatenate([far_a, far_b]), behind]
    else:
        parts = [block] + [lax.ppermute(block, "y", shift_pairs(y_n, d)) for d in range(1, y_n)]
    return jnp.stack(parts)


def body(resid_in, context, out_proj, norm_gain, router, routes, w_gate, w_up, w_down, next_gain):
    model_width = resid_in.shape[1]
    tokens = resid_in.shape[0]
    sizes = {a: lax.axis_size(a) for a in ("rep", "z", "y", "x")}
    rep_count = sizes["rep"]
    rep_id = lax.axis_index("rep")
    chip = ("z", "y", "x")

    gate_all = lax.all_gather(w_gate, "x", axis=1, tiled=True)
    up_all = lax.all_gather(w_up, "x", axis=1, tiled=True)
    down_all = lax.all_gather(w_down, "x", axis=0, tiled=True)

    token_ctx = lax.all_to_all(context, chip, split_axis=0, concat_axis=1, tiled=True)
    half = model_width // rep_count
    proj_half = lax.dynamic_slice_in_dim(out_proj, rep_id * half, half, axis=1)
    proj_rows = gather_proj(proj_half, sizes)
    feat_block = proj_half.shape[0]
    proj_rows = proj_rows.reshape(-1, half)
    dy = jnp.arange(sizes["y"])[:, None, None]
    dz = jnp.arange(sizes["z"])[None, :, None]
    dx = jnp.arange(sizes["x"])[None, None, :]
    src = (
        ((lax.axis_index("z") - dz) % sizes["z"]) * (sizes["y"] * sizes["x"])
        + ((lax.axis_index("y") - dy) % sizes["y"]) * sizes["x"]
        + (lax.axis_index("x") - dx) % sizes["x"]
    ).reshape(-1)
    chip_ctx = lax.all_gather(token_ctx, "rep", axis=0, tiled=True)
    chip_ctx = chip_ctx.reshape(chip_ctx.shape[0], -1, feat_block)
    chip_ctx = jnp.take(chip_ctx, src, axis=1).reshape(chip_ctx.shape[0], -1)
    att_cols = jnp.dot(chip_ctx, proj_rows, preferred_element_type=jnp.float32)
    att_full = lax.all_to_all(
        jnp.stack([att_cols] * rep_count), "rep", split_axis=0, concat_axis=2, tiled=True
    ).reshape(att_cols.shape[0], model_width)
    chip_resid = lax.all_gather(resid_in, "rep", axis=0, tiled=True)
    chip_routes = lax.all_gather(routes, "rep", axis=0, tiled=True)
    chip_hidden = (chip_resid.astype(jnp.float32) + att_full).astype(jnp.bfloat16)
    hidden = lax.dynamic_slice_in_dim(chip_hidden, rep_id * tokens, tokens, axis=0)
    chip_normed = rms_norm(chip_hidden, norm_gain)
    logits = jnp.dot(chip_normed, router, preferred_element_type=jnp.float32)
    experts = router.shape[1]
    picked_mask = (
        chip_routes[:, :, None] == jnp.arange(experts, dtype=jnp.int32)[None, None, :]
    ).astype(jnp.int32)
    picked = jnp.sum(picked_mask.astype(jnp.float32) * logits[:, None, :], axis=2)
    raised = jnp.exp(picked)
    chip_weight = (raised / jnp.sum(raised, axis=1, keepdims=True)).astype(jnp.bfloat16)

    named_count = jnp.sum(picked_mask, axis=1).reshape(rep_count, tokens, experts)
    before = (jnp.cumsum(named_count, axis=1) - named_count).reshape(rep_count * tokens, experts)
    rank_of = jnp.sum(picked_mask * before[:, None, :], axis=2)
    groups = experts // rep_count
    source_core = (jnp.arange(chip_routes.shape[0], dtype=jnp.int32) // tokens)[:, None]
    local_slot = jnp.where(
        chip_routes // groups == rep_id,
        ((chip_routes % groups) * MOST + rank_of) * rep_count + source_core,
        -1,
    )
    slot_total = groups * rep_count * MOST
    slot_hits = local_slot[None] == jnp.arange(slot_total, dtype=jnp.int32)[:, None, None]
    placing = jnp.any(slot_hits, axis=2).astype(jnp.bfloat16)
    outgoing = jnp.dot(placing, chip_normed, preferred_element_type=jnp.bfloat16)
    outgoing = outgoing.reshape(groups, MOST, rep_count, model_width)
    arrived = lax.all_to_all(outgoing, ("z", "y"), split_axis=0, concat_axis=0, tiled=True)
    rows = arrived.reshape(-1, model_width)

    block_size = w_gate.shape[1]
    quarters = sizes["x"]
    gate_h = jnp.dot(rows, gate_all, preferred_element_type=jnp.float32)
    up_h = jnp.dot(rows, up_all, preferred_element_type=jnp.float32)
    activated = (jax.nn.silu(gate_h) * up_h).astype(jnp.bfloat16)
    activated = activated.reshape(-1, quarters, block_size)
    produced = jnp.einsum(
        "sqj,qjd->sqd",
        activated,
        down_all.reshape(quarters, block_size, model_width),
        preferred_element_type=jnp.float32,
    ).astype(jnp.bfloat16)
    summed = jnp.sum(produced.astype(jnp.float32), axis=1).astype(jnp.bfloat16)
    summed = summed.reshape(arrived.shape)
    back = lax.all_to_all(summed, ("z", "y"), split_axis=0, concat_axis=0, tiled=True)
    back = back.reshape(slot_total, model_width)

    weighing = jnp.sum(
        slot_hits.astype(jnp.float32) * chip_weight.astype(jnp.float32)[None], axis=2
    ).T.astype(jnp.bfloat16)
    partial = jnp.dot(weighing, back, preferred_element_type=jnp.float32)
    partial = partial.reshape(rep_count, tokens, model_width)
    partial = lax.all_to_all(partial, "rep", split_axis=0, concat_axis=0, tiled=True)
    expert_sum = jnp.sum(partial, axis=0)
    resid_out = (hidden.astype(jnp.float32) + expert_sum).astype(jnp.bfloat16)
    next_normed = rms_norm(resid_out, next_gain)
    return (resid_out, next_normed)


def solution(mesh):
    rep_count = mesh.shape["rep"]
    ep_count = mesh.shape["ep"]
    units = 65536 // (rep_count * ep_count)
    owners = max(FF_E // units, 1)
    rows_of = 4 if (ep_count // owners) % 4 == 0 else 1
    devices = mesh.devices.reshape(rep_count, ep_count // owners // rows_of, rows_of, owners)
    grid = Mesh(devices, ("rep", "z", "y", "x"))
    tok = ("rep", "z", "y", "x")
    feat = ("z", "y", "x")
    in_specs = (
        P(tok, None),
        P("rep", feat),
        P(feat, None),
        P(),
        P(),
        P(tok, None),
        P(None, tok),
        P(None, tok),
        P(tok, None),
        P(),
    )
    out_specs = (P(tok, None), P(tok, None))
    return jax.shard_map(body, mesh=grid, in_specs=in_specs, out_specs=out_specs, check_vma=False)
```

```python
import jax
import jax.numpy as jnp
from jax import lax
from jax.sharding import Mesh
from jax.sharding import PartitionSpec as P

FF_E = 1024
MOST = 10


def rms_norm(values, gain_row):
    widened = values.astype(jnp.float32)
    factor = lax.rsqrt(jnp.mean(widened * widened, axis=-1, keepdims=True) + 1e-06)
    return (widened * factor * gain_row).astype(jnp.bfloat16)


def shift_pairs(size, offset):
    return [(i, (i + offset) % size) for i in range(size)]


def gather_proj(block, sizes):
    x_n, z_n, y_n = sizes["x"], sizes["z"], sizes["y"]
    parts = [block] + [lax.ppermute(block, "x", shift_pairs(x_n, d)) for d in range(1, x_n)]
    block = jnp.stack(parts)
    parts = [block] + [lax.ppermute(block, "z", shift_pairs(z_n, d)) for d in range(1, z_n)]
    block = jnp.stack(parts)
    if y_n == 4:
        ahead = lax.ppermute(block, "y", shift_pairs(4, 1))
        behind = lax.ppermute(block, "y", shift_pairs(4, 3))
        cut = block.shape[0] // 2
        far_a = lax.ppermute(ahead[:cut], "y", shift_pairs(4, 1))
        far_b = lax.ppermute(behind[cut:], "y", shift_pairs(4, 3))
        parts = [block, ahead, jnp.concatenate([far_a, far_b]), behind]
    else:
        parts = [block] + [lax.ppermute(block, "y", shift_pairs(y_n, d)) for d in range(1, y_n)]
    return jnp.stack(parts)


def body(resid_in, context, out_proj, norm_gain, router, routes, w_gate, w_up, w_down, next_gain):
    model_width = resid_in.shape[1]
    tokens = resid_in.shape[0]
    sizes = {a: lax.axis_size(a) for a in ("rep", "z", "y", "x")}
    rep_count = sizes["rep"]
    rep_id = lax.axis_index("rep")
    chip = ("z", "y", "x")

    gate_all = lax.all_gather(w_gate, "x", axis=1, tiled=True)
    up_all = lax.all_gather(w_up, "x", axis=1, tiled=True)
    down_all = lax.all_gather(w_down, "x", axis=0, tiled=True)

    token_ctx = lax.all_to_all(context, chip, split_axis=0, concat_axis=1, tiled=True)
    half = model_width // rep_count
    proj_half = lax.dynamic_slice_in_dim(out_proj, rep_id * half, half, axis=1)
    proj_rows = gather_proj(proj_half, sizes)
    feat_block = proj_half.shape[0]
    proj_rows = proj_rows.reshape(-1, half)
    dy = jnp.arange(sizes["y"])[:, None, None]
    dz = jnp.arange(sizes["z"])[None, :, None]
    dx = jnp.arange(sizes["x"])[None, None, :]
    src = (
        ((lax.axis_index("z") - dz) % sizes["z"]) * (sizes["y"] * sizes["x"])
        + ((lax.axis_index("y") - dy) % sizes["y"]) * sizes["x"]
        + (lax.axis_index("x") - dx) % sizes["x"]
    ).reshape(-1)
    chip_ctx = lax.all_gather(token_ctx, "rep", axis=0, tiled=True)
    chip_ctx = chip_ctx.reshape(chip_ctx.shape[0], -1, feat_block)
    chip_ctx = jnp.take(chip_ctx, src, axis=1).reshape(chip_ctx.shape[0], -1)
    att_cols = jnp.dot(chip_ctx, proj_rows, preferred_element_type=jnp.float32)
    att_cols = att_cols.reshape(rep_count, tokens, half).astype(jnp.bfloat16)
    attention = lax.all_to_all(att_cols, "rep", split_axis=0, concat_axis=2, tiled=True)
    attention = attention.reshape(tokens, model_width).astype(jnp.float32)

    hidden = (resid_in.astype(jnp.float32) + attention).astype(jnp.bfloat16)
    normed = rms_norm(hidden, norm_gain)
    logits = jnp.dot(normed, router, preferred_element_type=jnp.float32)
    experts = router.shape[1]
    picked_mask = (
        routes[:, :, None] == jnp.arange(experts, dtype=jnp.int32)[None, None, :]
    ).astype(jnp.int32)
    picked = jnp.sum(picked_mask.astype(jnp.float32) * logits[:, None, :], axis=2)
    raised = jnp.exp(picked)
    route_weight = (raised / jnp.sum(raised, axis=1, keepdims=True)).astype(jnp.bfloat16)

    named_count = jnp.sum(picked_mask, axis=1)
    before = jnp.cumsum(named_count, axis=0) - named_count
    order_rank = jnp.sum(picked_mask * before[:, None, :], axis=2)
    groups = experts // rep_count
    slot_index = ((routes % groups) * rep_count + routes // groups) * MOST + order_rank
    chip_slot = lax.all_gather(slot_index, "rep", axis=0, tiled=True)
    chip_weight = lax.all_gather(route_weight, "rep", axis=0, tiled=True)
    chip_normed = lax.all_gather(normed, "rep", axis=0, tiled=True)
    source_core = (jnp.arange(chip_slot.shape[0], dtype=jnp.int32) // tokens)[:, None]
    group_of = chip_slot // (rep_count * MOST)
    core_of = (chip_slot // MOST) % rep_count
    rank_of = chip_slot % MOST
    local_slot = jnp.where(
        core_of == rep_id, (group_of * MOST + rank_of) * rep_count + source_core, -1
    )
    slot_total = groups * rep_count * MOST
    slot_hits = local_slot[None] == jnp.arange(slot_total, dtype=jnp.int32)[:, None, None]
    placing = jnp.any(slot_hits, axis=2).astype(jnp.bfloat16)
    outgoing = jnp.dot(placing, chip_normed, preferred_element_type=jnp.bfloat16)
    outgoing = outgoing.reshape(groups, MOST, rep_count, model_width)
    arrived = lax.all_to_all(outgoing, ("z", "y"), split_axis=0, concat_axis=0, tiled=True)
    rows = arrived.reshape(-1, model_width)

    block_size = w_gate.shape[1]
    quarters = sizes["x"]
    gate_h = jnp.dot(rows, gate_all, preferred_element_type=jnp.float32)
    up_h = jnp.dot(rows, up_all, preferred_element_type=jnp.float32)
    activated = (jax.nn.silu(gate_h) * up_h).astype(jnp.bfloat16)
    activated = activated.reshape(-1, quarters, block_size)
    produced = jnp.einsum(
        "sqj,qjd->sqd",
        activated,
        down_all.reshape(quarters, block_size, model_width),
        preferred_element_type=jnp.float32,
    ).astype(jnp.bfloat16)
    summed = jnp.sum(produced.astype(jnp.float32), axis=1).astype(jnp.bfloat16)
    summed = summed.reshape(arrived.shape)
    back = lax.all_to_all(summed, ("z", "y"), split_axis=0, concat_axis=0, tiled=True)
    back = back.reshape(slot_total, model_width)

    weighing = jnp.sum(
        slot_hits.astype(jnp.float32) * chip_weight.astype(jnp.float32)[None], axis=2
    ).T.astype(jnp.bfloat16)
    partial = jnp.dot(weighing, back, preferred_element_type=jnp.float32)
    partial = partial.reshape(rep_count, tokens, model_width).astype(jnp.bfloat16)
    partial = lax.all_to_all(partial, "rep", split_axis=0, concat_axis=0, tiled=True)
    expert_sum = jnp.sum(partial.astype(jnp.float32), axis=0)
    resid_out = (hidden.astype(jnp.float32) + expert_sum).astype(jnp.bfloat16)
    next_normed = rms_norm(resid_out, next_gain)
    return (resid_out, next_normed)


def solution(mesh):
    rep_count = mesh.shape["rep"]
    ep_count = mesh.shape["ep"]
    units = 65536 // (rep_count * ep_count)
    owners = max(FF_E // units, 1)
    rows_of = 4 if (ep_count // owners) % 4 == 0 else 1
    devices = mesh.devices.reshape(rep_count, ep_count // owners // rows_of, rows_of, owners)
    grid = Mesh(devices, ("rep", "z", "y", "x"))
    tok = ("rep", "z", "y", "x")
    feat = ("z", "y", "x")
    in_specs = (
        P(tok, None),
        P("rep", feat),
        P(feat, None),
        P(),
        P(),
        P(tok, None),
        P(None, tok),
        P(None, tok),
        P(tok, None),
        P(),
    )
    out_specs = (P(tok, None), P(tok, None))
    return jax.shard_map(body, mesh=grid, in_specs=in_specs, out_specs=out_specs, check_vma=False)
```
